256 devices in a mesh: dp: 128 (over y, z, x_lo, core), rows: 2 (over x_hi).
Axes of the slice: x: 4 (x_hi: 2, x_lo: 2; x = x_hi * 2 + x_lo), y: 4, z: 8, core: 2. Of those that a mesh axis runs over, the one named last changes fastest.
Arguments:
- features: bfloat16 [128, 32, 32, 768], P('dp', 'rows'), may hold values from -24 to 24
- bucket: int32 [128], P('dp'), may hold values from 0 to 16, as said below
- kernel: float32 [7, 7, 768], replicated, may hold values from -0.875 to 0.875
- up_weight: bfloat16 [768, 2816], P('dp'), may hold values from -0.21875 to 0.21875
- down_weight: bfloat16 [2816, 768], P('dp'), may hold values from -0.109375 to 0.109375
- cotangent: bfloat16 [128, 32, 32, 768], P('dp', 'rows'), may hold values from -6 to 6
Outputs:
- block_out: bfloat16 [128, 32, 32, 768], P('dp', 'rows')
- feature_grad: bfloat16 [128, 32, 32, 768], P('dp', 'rows')
- up_grad: float32 [768, 2816], P('dp')
- down_grad: float32 [2816, 768], P('dp')
- kernel_grad: float32 [7, 7, 768], replicated
The draws below stay inside these ranges and needn't reach their ends.
Inputs may be any that keep to these rules, and one draw needn't show every extreme that they name: `bucket`: both ends of the range occur in every draw.
All inputs are finite; a program needn't handle non-finite values.
Results may differ from the reference program's by a relative error of at most 0.0075.
Values may be sent and summed in bfloat16 or wider, within the bound.
No kernel may reach another device: no remote copies, remote signals or barrier semaphores. Data moves between devices by JAX's collectives and lax.ppermute only.
A program may use at most 128 MiB of HBM per device.

```python
import jax
import jax.numpy as jnp
from jax import lax

C = 768
HID = 2816
KS = 7
CH = 32
CW = 32
IMAGES = 128
AREA = 512


def draw_bucket(key, part):
    first_key, second_key = jax.random.split(jax.random.fold_in(key, 11))
    drawn = jax.random.randint(first_key, (IMAGES,), 0, CH // 2 + 1)
    ranking = jax.random.permutation(second_key, IMAGES)
    drawn = jnp.where(ranking == 0, 0, drawn)
    drawn = jnp.where(ranking == 1, CH // 2, drawn)
    return drawn.astype(jnp.int32)


def strengthened(values, own_key, source, target, parts, factor):
    owner, partner = [(jnp.arange(values.shape[dim]) // (values.shape[dim] // parts)).reshape([-1 if axis == dim else 1 for axis in range(values.ndim)]) for dim in (source, target)]
    chosen = jax.random.permutation(own_key, parts)[partner]
    strong = (owner == chosen) | (owner == (partner + parts // 2) % parts)
    return jnp.where(strong, factor * values, values)


def level_of(stream_key, extent, cuts, least, high):
    gain, own = 1.0, jax.random.fold_in(stream_key, 6)
    for axis_at, shards_of in cuts:
        draws = jnp.exp(jax.random.uniform(jax.random.fold_in(own, axis_at), (shards_of,), jnp.float32, least / len(cuts), high / len(cuts)))
        gain = gain * jnp.repeat(draws, extent[axis_at] // shards_of).reshape([-1 if axis == axis_at else 1 for axis in range(len(extent))])
    return gain


def centred(key, extent, spread, most, cuts=(), held_as=jnp.bfloat16):
    array = jax.random.normal(key, extent, jnp.float32) * spread
    if len(cuts) > 0:
        array = level_of(key, extent, cuts, -0.22, 0.18) * array
    return jnp.clip(array, min=-most, max=most).astype(held_as)


def heavy_noise(stream_key, dims, deviation, most, cuts, heavy, held_as=jnp.bfloat16):
    values = deviation * jax.random.normal(stream_key, dims, jnp.float32)
    if cuts:
        values = values * level_of(stream_key, dims, cuts, -0.22, 0.18)
    return jnp.clip(strengthened(values, jax.random.fold_in(stream_key, 3), *heavy), -most, most).astype(held_as)


def setup_inputs(seed: int = 0) -> dict:
    key_list = jax.random.split(jax.random.key(seed), 7)
    return {
        "features": heavy_noise(key_list[0], (IMAGES, CH, CW, C), 1.0, 24.0, ((0, 128), (1, 2)), (0, 3, 128, 5.5)),
        "bucket": draw_bucket(jax.random.fold_in(key_list[6], 71), 0),
        "kernel": centred(key_list[2], (KS, KS, C), (KS * KS) ** -0.5, 0.875, (), jnp.float32),
        "up_weight": centred(key_list[3], (C, HID), C ** -0.5, 0.21875, ((0, 128),)),
        "down_weight": centred(key_list[4], (HID, C), HID ** -0.5, 0.109375, ((0, 128),)),
        "cotangent": centred(key_list[5], (IMAGES, CH, CW, C), 1.0, 6.0, ((0, 128), (1, 2))),
    }


INV_ROOT_TWO = 0.7071067811865476
INV_ROOT_TAU = 0.3989422804014327
EPSILON = 1e-06

def gelu_parts(pre_act):
    normal_cdf = 0.5 * (1.0 + lax.erf(pre_act * INV_ROOT_TWO))
    density = jnp.exp(-0.5 * pre_act * pre_act) * INV_ROOT_TAU
    return (pre_act * normal_cdf, normal_cdf + pre_act * density)

def depthwise(padded, kernel, out_rows, out_cols, flipped):
    span = kernel.shape[0]
    result = jnp.zeros(padded.shape[:-3] + (out_rows, out_cols, padded.shape[-1]), jnp.float32)
    for offset_row in range(span):
        for offset_col in range(span):
            start_row = span - 1 - offset_row if flipped else offset_row
            start_col = span - 1 - offset_col if flipped else offset_col
            result = result + kernel[offset_row, offset_col] * padded[..., start_row:start_row + out_rows, start_col:start_col + out_cols, :]
    return result

def kernel_terms(grad_conv, padded, span):
    reduce_axes = tuple(range(grad_conv.ndim - 1))
    rows_out = grad_conv.shape[-3]
    cols_out = grad_conv.shape[-2]
    kernel_rows = []
    for offset_row in range(span):
        kernel_row = []
        for offset_col in range(span):
            window = padded[..., offset_row:offset_row + rows_out, offset_col:offset_col + cols_out, :]
            kernel_row.append(lax.optimization_barrier(jnp.sum(grad_conv * window, axis=reduce_axes)))
        kernel_rows.append(jnp.stack(kernel_row))
    return jnp.stack(kernel_rows)

def layer_norm(convolved):
    centered = convolved - lax.optimization_barrier(jnp.mean(convolved, axis=-1, keepdims=True))
    inv_std = lax.rsqrt(lax.optimization_barrier(jnp.mean(centered * centered, axis=-1, keepdims=True)) + EPSILON)
    return (centered * inv_std, inv_std)

def norm_backward(grad_norm, unit_norm, inv_std):
    first_mean = lax.optimization_barrier(jnp.mean(grad_norm, axis=-1, keepdims=True))
    second_mean = lax.optimization_barrier(jnp.mean(grad_norm * unit_norm, axis=-1, keepdims=True))
    return inv_std * (grad_norm - first_mean - unit_norm * second_mean)

def pointwise(tokens, cot_rows, up_full, down_full):
    pre_act = jnp.dot(tokens, up_full, preferred_element_type=jnp.float32)
    hidden, derivative = gelu_parts(pre_act)
    activation = hidden.astype(jnp.bfloat16)
    branch = jnp.dot(activation, down_full, preferred_element_type=jnp.float32)
    grad_act = lax.dot_general(cot_rows, down_full, (((1,), (1,)), ((), ())), preferred_element_type=jnp.float32)
    grad_pre = (grad_act * derivative).astype(jnp.bfloat16)
    grad_norm = lax.dot_general(grad_pre, up_full, (((1,), (1,)), ((), ())), preferred_element_type=jnp.float32)
    return (activation, branch, grad_pre, grad_norm)

def reference(features, bucket, kernel, up_weight, down_weight, cotangent):
    reach = KS // 2

    def one_image(carry, inputs):
        feature_one, cot_one, bucket_one = inputs
        image_rows = CH // 2 + bucket_one
        image_cols = jnp.minimum(CW, AREA // image_rows)
        inside = (jnp.arange(CH, dtype=jnp.int32)[:, None] < image_rows) & (jnp.arange(CW, dtype=jnp.int32)[None, :] < image_cols)
        inside_cells = inside[:, :, None]
        masked = jnp.where(inside_cells, feature_one, jnp.zeros((), feature_one.dtype))
        masked_cot = jnp.where(inside_cells, cot_one, jnp.zeros((), cot_one.dtype))
        padded = jnp.pad(masked, ((reach, reach), (reach, reach), (0, 0)))
        convolved = jnp.where(inside_cells, depthwise(padded, kernel, CH, CW, False), 0.0)
        unit_norm, inv_std = layer_norm(convolved)
        normed = unit_norm.astype(jnp.bfloat16)
        tokens = normed.reshape(CH * CW, C)
        cot_rows = masked_cot.reshape(CH * CW, C)
        activation, branch, grad_pre, grad_norm = pointwise(tokens, cot_rows, up_weight, down_weight)
        block_out = (masked + branch.reshape(CH, CW, C)).astype(jnp.bfloat16)
        down_term = lax.dot_general(activation, cot_rows, (((0,), (0,)), ((), ())), preferred_element_type=jnp.float32)
        up_term = lax.dot_general(tokens, grad_pre, (((0,), (0,)), ((), ())), preferred_element_type=jnp.float32)
        grad_conv = jnp.where(inside_cells, norm_backward(grad_norm.reshape(CH, CW, C), unit_norm, inv_std), 0.0)
        kernel_term = kernel_terms(grad_conv, padded, KS)
        grad_padded = jnp.pad(grad_conv, ((reach, reach), (reach, reach), (0, 0)))
        feature_grad = jnp.where(inside_cells, masked_cot + depthwise(grad_padded, kernel, CH, CW, True), 0.0).astype(jnp.bfloat16)
        new_carry = (carry[0] + down_term, carry[1] + up_term, carry[2] + kernel_term)
        return (new_carry, (block_out, feature_grad))
    start = (jnp.zeros((HID, C), jnp.float32), jnp.zeros((C, HID), jnp.float32), jnp.zeros((KS, KS, C), jnp.float32))
    totals, outputs = lax.scan(one_image, start, (features, cotangent, bucket))
    block_out, feature_grad = outputs
    return (block_out, feature_grad, totals[1] / IMAGES, totals[0] / IMAGES, totals[2] / IMAGES)
```

```python
import jax
import jax.numpy as jnp
from jax import lax
from jax.sharding import Mesh
from jax.sharding import PartitionSpec as P

INV_ROOT_TWO = 0.7071067811865476
INV_ROOT_TAU = 0.3989422804014327
EPSILON = 1e-06

AXES = ("y", "z", "xl", "c", "rows")
SIZES = (4, 8, 2, 2, 2)
DP = AXES[:4]
SIZE = dict(zip(AXES, SIZES))


def ring_gather(x, axis):
    n = SIZE[axis]
    me = lax.axis_index(axis)
    m = x.shape[0]
    out = jnp.zeros((n * m,) + x.shape[1:], x.dtype)
    out = lax.dynamic_update_slice_in_dim(out, x, me * m, 0)
    right = n // 2
    left = n - 1 - right
    cur = x
    for s in range(1, right + 1):
        cur = lax.ppermute(cur, axis, [(i, (i + 1) % n) for i in range(n)])
        out = lax.dynamic_update_slice_in_dim(out, cur, ((me - s) % n) * m, 0)
    cur = x
    for s in range(1, left + 1):
        cur = lax.ppermute(cur, axis, [(i, (i - 1) % n) for i in range(n)])
        out = lax.dynamic_update_slice_in_dim(out, cur, ((me + s) % n) * m, 0)
    return out


def ring_scatter(x, axis, wire):
    n = SIZE[axis]
    me = lax.axis_index(axis)
    m = x.shape[0] // n

    def block(j):
        return lax.dynamic_slice_in_dim(x, (j % n) * m, m, 0)

    if n == 2:
        got = lax.ppermute(block(me + 1).astype(wire), axis, [(0, 1), (1, 0)])
        return block(me) + got.astype(jnp.float32)
    half = x.shape[1] // 2
    acc_r = block(me - 1)[:, :half]
    acc_l = block(me + 1)[:, half:]
    for s in range(1, n):
        got_r = lax.ppermute(acc_r.astype(wire), axis, [(i, (i + 1) % n) for i in range(n)])
        got_l = lax.ppermute(acc_l.astype(wire), axis, [(i, (i - 1) % n) for i in range(n)])
        j_r, j_l = (me - s - 1, me + s + 1) if s < n - 1 else (me, me)
        acc_r = got_r.astype(jnp.float32) + block(j_r)[:, :half]
        acc_l = got_l.astype(jnp.float32) + block(j_l)[:, half:]
    return jnp.concatenate([acc_r, acc_l], axis=1)


def gather_weight(shard):
    rows = shard.shape[0]
    for axis in ("c", "xl", "y", "z"):
        shard = ring_gather(shard, axis)
    shard = shard.reshape(SIZE["z"], SIZE["y"], -1, shard.shape[1]).transpose(1, 0, 2, 3)
    return shard.reshape(-1, shard.shape[3])


def reduce_weight_grad(term):
    order = ("c", "z", "y", "xl")
    n = term.shape[0]
    tiles = term.reshape(*SIZES[:4], n // 128, term.shape[1])
    tiles = tiles.transpose([DP.index(a) for a in order] + [4, 5]).reshape(n, -1)
    for axis in order:
        tiles = ring_scatter(tiles, axis, jnp.bfloat16)
    return tiles + lax.ppermute(tiles, "rows", [(0, 1), (1, 0)])


def padded_2(block, sides, width):
    for axis, dim in sides:
        count = lax.axis_size(axis)
        forward = [(i, i + 1) for i in range(count - 1)]
        backward = [(target, source) for source, target in forward]
        low = lax.ppermute(
            lax.slice_in_dim(block, block.shape[dim] - width, None, axis=dim), axis, forward
        )
        high = lax.ppermute(lax.slice_in_dim(block, 0, width, axis=dim), axis, backward)
        block = jnp.concatenate([low, block, high], axis=dim)
    return block


def gelu_parts(pre_act):
    normal_cdf = 0.5 * (1.0 + lax.erf(pre_act * INV_ROOT_TWO))
    density = jnp.exp(-0.5 * pre_act * pre_act) * INV_ROOT_TAU
    return (pre_act * normal_cdf, normal_cdf + pre_act * density)


def depthwise(padded, kernel, out_rows, out_cols, flipped):
    span = kernel.shape[0]
    result = jnp.zeros(padded.shape[:-3] + (out_rows, out_cols, padded.shape[-1]), jnp.float32)
    for offset_row in range(span):
        for offset_col in range(span):
            start_row = span - 1 - offset_row if flipped else offset_row
            start_col = span - 1 - offset_col if flipped else offset_col
            result = (
                result
                + kernel[offset_row, offset_col]
                * padded[..., start_row : start_row + out_rows, start_col : start_col + out_cols, :]
            )
    return result


def kernel_terms(grad_conv, padded, span):
    reduce_axes = tuple(range(grad_conv.ndim - 1))
    rows_out = grad_conv.shape[-3]
    cols_out = grad_conv.shape[-2]
    kernel_rows = []
    for offset_row in range(span):
        kernel_row = []
        for offset_col in range(span):
            window = padded[
                ..., offset_row : offset_row + rows_out, offset_col : offset_col + cols_out, :
            ]
            kernel_row.append(jnp.sum(grad_conv * window, axis=reduce_axes))
        kernel_rows.append(jnp.stack(kernel_row))
    return jnp.stack(kernel_rows)


def layer_norm(convolved):
    centered = convolved - jnp.mean(convolved, axis=-1, keepdims=True)
    inv_std = lax.rsqrt(jnp.mean(centered * centered, axis=-1, keepdims=True) + EPSILON)
    return (centered * inv_std, inv_std)


def norm_backward(grad_norm, unit_norm, inv_std):
    first_mean = jnp.mean(grad_norm, axis=-1, keepdims=True)
    second_mean = jnp.mean(grad_norm * unit_norm, axis=-1, keepdims=True)
    return inv_std * (grad_norm - first_mean - unit_norm * second_mean)


def on_device(features, bucket, kernel, up_weight, down_weight, cotangent):
    images, strip_rows, canvas_cols, channels = features.shape
    rows_count = lax.axis_size("rows")
    row_index = lax.axis_index("rows")
    canvas_rows = strip_rows * rows_count
    area_cells = canvas_rows * canvas_cols // 2
    reach = kernel.shape[0] // 2
    grad_scale = 1.0 / (images * lax.axis_size(DP))
    heights = canvas_rows // 2 + bucket
    widths = jnp.minimum(canvas_cols, area_cells // heights)
    row_ids = row_index * strip_rows + lax.iota(jnp.int32, strip_rows)
    col_ids = lax.iota(jnp.int32, canvas_cols)
    inside = (row_ids[None, :, None] < heights[:, None, None]) & (
        col_ids[None, None, :] < widths[:, None, None]
    )
    inside_cells = inside[..., None]
    masked = jnp.where(inside_cells, features, jnp.zeros((), features.dtype))
    masked_cot = jnp.where(inside_cells, cotangent, jnp.zeros((), cotangent.dtype))
    up_full = gather_weight(up_weight)
    down_full = gather_weight(down_weight)
    rimmed = padded_2(masked, (("rows", 1),), reach)
    padded = jnp.pad(rimmed, ((0, 0), (0, 0), (reach, reach), (0, 0)))
    convolved = jnp.where(
        inside_cells, depthwise(padded, kernel, strip_rows, canvas_cols, False), 0.0
    )
    unit_norm, inv_std = layer_norm(convolved)
    normed = unit_norm.astype(jnp.bfloat16)
    tokens = normed.reshape(images * strip_rows * canvas_cols, channels)
    cot_rows = masked_cot.reshape(images * strip_rows * canvas_cols, channels)

    pre_act = jnp.dot(tokens, up_full, preferred_element_type=jnp.float32)
    hidden, derivative = gelu_parts(pre_act)
    activation = hidden.astype(jnp.bfloat16)
    down_term = lax.dot_general(
        activation, cot_rows, (((0,), (0,)), ((), ())), preferred_element_type=jnp.float32
    )
    down_grad = reduce_weight_grad(down_term * grad_scale)
    branch = jnp.dot(activation, down_full, preferred_element_type=jnp.float32)
    grad_act = lax.dot_general(
        cot_rows, down_full, (((1,), (1,)), ((), ())), preferred_element_type=jnp.float32
    )
    grad_pre = (grad_act * derivative).astype(jnp.bfloat16)
    up_term = lax.dot_general(
        tokens, grad_pre, (((0,), (0,)), ((), ())), preferred_element_type=jnp.float32
    )
    up_grad = reduce_weight_grad(up_term * grad_scale)
    grad_rows = lax.dot_general(
        grad_pre, up_full, (((1,), (1,)), ((), ())), preferred_element_type=jnp.float32
    )

    branch = branch.reshape(features.shape)
    grad_norm = grad_rows.reshape(features.shape)
    block_out = (masked + branch).astype(jnp.bfloat16)
    grad_conv = jnp.where(inside_cells, norm_backward(grad_norm, unit_norm, inv_std), 0.0)
    kernel_grad = lax.psum(
        kernel_terms(grad_conv, padded, kernel.shape[0]) * grad_scale, AXES
    )
    grad_rimmed = padded_2(grad_conv.astype(jnp.bfloat16), (("rows", 1),), reach).astype(
        grad_conv.dtype
    )
    grad_padded = jnp.pad(grad_rimmed, ((0, 0), (0, 0), (reach, reach), (0, 0)))
    feature_grad = jnp.where(
        inside_cells,
        masked_cot + depthwise(grad_padded, kernel, strip_rows, canvas_cols, True),
        0.0,
    ).astype(jnp.bfloat16)
    return (block_out, feature_grad, up_grad, down_grad, kernel_grad)


def solution(mesh):
    torus = Mesh(mesh.devices.reshape(SIZES), AXES)
    strips = P(DP, "rows", None, None)
    return jax.shard_map(
        on_device,
        mesh=torus,
        in_specs=(strips, P(DP), P(), P(DP, None), P(DP, None), strips),
        out_specs=(strips, strips, P(DP, None), P(DP, None), P()),
        check_vma=False,
    )
```

```python
import jax
import jax.numpy as jnp
from jax import lax
from jax.sharding import Mesh
from jax.sharding import PartitionSpec as P

INV_ROOT_TWO = 0.7071067811865476
INV_ROOT_TAU = 0.3989422804014327
EPSILON = 1e-06

AXES = ("y", "z", "xl", "c", "rows")
SIZES = (4, 8, 2, 2, 2)
DP = AXES[:4]
SIZE = dict(zip(AXES, SIZES))


def ring_gather(x, axis):
    n = SIZE[axis]
    me = lax.axis_index(axis)
    dim = AXES.index(axis)
    shape = list(x.shape)
    shape[dim] = n
    out = jnp.zeros(shape, x.dtype)
    out = lax.dynamic_update_slice_in_dim(out, x, me, dim)
    right = n // 2
    left = n - 1 - right
    cur = x
    for s in range(1, right + 1):
        cur = lax.ppermute(cur, axis, [(i, (i + 1) % n) for i in range(n)])
        out = lax.dynamic_update_slice_in_dim(out, cur, (me - s) % n, dim)
    cur = x
    for s in range(1, left + 1):
        cur = lax.ppermute(cur, axis, [(i, (i - 1) % n) for i in range(n)])
        out = lax.dynamic_update_slice_in_dim(out, cur, (me + s) % n, dim)
    return out


def ring_scatter(x, axis, wire):
    n = SIZE[axis]
    me = lax.axis_index(axis)
    dim = AXES.index(axis)

    def block(j):
        return lax.dynamic_slice_in_dim(x, j % n, 1, dim)

    if n == 2:
        got = lax.ppermute(block(me + 1).astype(wire), axis, [(0, 1), (1, 0)])
        return block(me) + got.astype(jnp.float32)
    half = x.shape[-1] // 2
    acc_r = block(me - 1)[..., :half]
    acc_l = block(me + 1)[..., half:]
    for s in range(1, n):
        got_r = lax.ppermute(acc_r.astype(wire), axis, [(i, (i + 1) % n) for i in range(n)])
        got_l = lax.ppermute(acc_l.astype(wire), axis, [(i, (i - 1) % n) for i in range(n)])
        j_r, j_l = (me - s - 1, me + s + 1) if s < n - 1 else (me, me)
        acc_r = got_r.astype(jnp.float32) + block(j_r)[..., :half]
        acc_l = got_l.astype(jnp.float32) + block(j_l)[..., half:]
    return jnp.concatenate([acc_r, acc_l], axis=-1)


def gather_weight(shard, order):
    rows, cols = shard.shape
    view = shard.reshape(1, 1, 1, 1, 1, rows, cols)
    for axis in order:
        view = ring_gather(view, axis)
    return view.reshape(-1, cols)


def reduce_weight_grad(term, order):
    rows = term.shape[0] // 128
    view = term.reshape(*SIZES[:4], 1, rows, term.shape[1])
    for axis in order:
        view = ring_scatter(view, axis, jnp.bfloat16)
    tiles = view.reshape(rows, term.shape[1])
    return tiles + lax.ppermute(tiles, "rows", [(0, 1), (1, 0)])


def butterfly_sum(x):
    for axis, n in zip(AXES, SIZES):
        d = 1
        while d < n:
            x = x + lax.ppermute(x, axis, [(i, i ^ d) for i in range(n)])
            d *= 2
    return x


def padded_2(block, sides, width):
    for axis, dim in sides:
        count = lax.axis_size(axis)
        forward = [(i, i + 1) for i in range(count - 1)]
        backward = [(target, source) for source, target in forward]
        low = lax.ppermute(
            lax.slice_in_dim(block, block.shape[dim] - width, None, axis=dim), axis, forward
        )
        high = lax.ppermute(lax.slice_in_dim(block, 0, width, axis=dim), axis, backward)
        block = jnp.concatenate([low, block, high], axis=dim)
    return block


def gelu_parts(pre_act):
    normal_cdf = 0.5 * (1.0 + lax.erf(pre_act * INV_ROOT_TWO))
    density = jnp.exp(-0.5 * pre_act * pre_act) * INV_ROOT_TAU
    return (pre_act * normal_cdf, normal_cdf + pre_act * density)


def depthwise(padded, kernel, out_rows, out_cols, flipped):
    span = kernel.shape[0]
    result = jnp.zeros(padded.shape[:-3] + (out_rows, out_cols, padded.shape[-1]), jnp.float32)
    for offset_row in range(span):
        for offset_col in range(span):
            start_row = span - 1 - offset_row if flipped else offset_row
            start_col = span - 1 - offset_col if flipped else offset_col
            result = (
                result
                + kernel[offset_row, offset_col]
                * padded[..., start_row : start_row + out_rows, start_col : start_col + out_cols, :]
            )
    return result


def kernel_terms(grad_conv, padded, span):
    reduce_axes = tuple(range(grad_conv.ndim - 1))
    rows_out = grad_conv.shape[-3]
    cols_out = grad_conv.shape[-2]
    kernel_rows = []
    for offset_row in range(span):
        kernel_row = []
        for offset_col in range(span):
            window = padded[
                ..., offset_row : offset_row + rows_out, offset_col : offset_col + cols_out, :
            ]
            kernel_row.append(jnp.sum(grad_conv * window, axis=reduce_axes))
        kernel_rows.append(jnp.stack(kernel_row))
    return jnp.stack(kernel_rows)


def layer_norm(convolved):
    centered = convolved - jnp.mean(convolved, axis=-1, keepdims=True)
    inv_std = lax.rsqrt(jnp.mean(centered * centered, axis=-1, keepdims=True) + EPSILON)
    return (centered * inv_std, inv_std)


def norm_backward(grad_norm, unit_norm, inv_std):
    first_mean = jnp.mean(grad_norm, axis=-1, keepdims=True)
    second_mean = jnp.mean(grad_norm * unit_norm, axis=-1, keepdims=True)
    return inv_std * (grad_norm - first_mean - unit_norm * second_mean)


def on_device(features, bucket, kernel, up_weight, down_weight, cotangent):
    images, strip_rows, canvas_cols, channels = features.shape
    rows_count = lax.axis_size("rows")
    row_index = lax.axis_index("rows")
    canvas_rows = strip_rows * rows_count
    area_cells = canvas_rows * canvas_cols // 2
    reach = kernel.shape[0] // 2
    grad_scale = 1.0 / (images * lax.axis_size(DP))
    heights = canvas_rows // 2 + bucket
    widths = jnp.minimum(canvas_cols, area_cells // heights)
    row_ids = row_index * strip_rows + lax.iota(jnp.int32, strip_rows)
    col_ids = lax.iota(jnp.int32, canvas_cols)
    inside = (row_ids[None, :, None] < heights[:, None, None]) & (
        col_ids[None, None, :] < widths[:, None, None]
    )
    inside_cells = inside[..., None]
    masked = jnp.where(inside_cells, features, jnp.zeros((), features.dtype))
    masked_cot = jnp.where(inside_cells, cotangent, jnp.zeros((), cotangent.dtype))
    up_full = gather_weight(up_weight, ("xl", "y", "z", "c"))
    down_full = gather_weight(down_weight, ("xl", "z", "y", "c"))
    rimmed = padded_2(masked, (("rows", 1),), reach)
    padded = jnp.pad(rimmed, ((0, 0), (0, 0), (reach, reach), (0, 0)))
    convolved = jnp.where(
        inside_cells, depthwise(padded, kernel, strip_rows, canvas_cols, False), 0.0
    )
    unit_norm, inv_std = layer_norm(convolved)
    normed = unit_norm.astype(jnp.bfloat16)
    tokens = normed.reshape(images * strip_rows * canvas_cols, channels)
    cot_rows = masked_cot.reshape(images * strip_rows * canvas_cols, channels)

    pre_act = jnp.dot(tokens, up_full, preferred_element_type=jnp.float32)
    hidden, derivative = gelu_parts(pre_act)
    activation = hidden.astype(jnp.bfloat16)
    down_term = lax.dot_general(
        activation, cot_rows, (((0,), (0,)), ((), ())), preferred_element_type=jnp.float32
    )
    down_grad = reduce_weight_grad(down_term * grad_scale, ("c", "y", "z", "xl"))
    branch = jnp.dot(activation, down_full, preferred_element_type=jnp.float32)
    grad_act = lax.dot_general(
        cot_rows, down_full, (((1,), (1,)), ((), ())), preferred_element_type=jnp.float32
    )
    grad_pre = (grad_act * derivative).astype(jnp.bfloat16)
    up_term = lax.dot_general(
        tokens, grad_pre, (((0,), (0,)), ((), ())), preferred_element_type=jnp.float32
    )
    up_grad = reduce_weight_grad(up_term * grad_scale, ("c", "z", "y", "xl"))
    grad_rows = lax.dot_general(
        grad_pre, up_full, (((1,), (1,)), ((), ())), preferred_element_type=jnp.float32
    )

    branch = branch.reshape(features.shape)
    grad_norm = grad_rows.reshape(features.shape)
    block_out = (masked + branch).astype(jnp.bfloat16)
    grad_conv = jnp.where(inside_cells, norm_backward(grad_norm, unit_norm, inv_std), 0.0)
    kernel_grad = butterfly_sum(kernel_terms(grad_conv, padded, kernel.shape[0]) * grad_scale)
    grad_rimmed = padded_2(grad_conv.astype(jnp.bfloat16), (("rows", 1),), reach).astype(
        grad_conv.dtype
    )
    grad_padded = jnp.pad(grad_rimmed, ((0, 0), (0, 0), (reach, reach), (0, 0)))
    feature_grad = jnp.where(
        inside_cells,
        masked_cot + depthwise(grad_padded, kernel, strip_rows, canvas_cols, True),
        0.0,
    ).astype(jnp.bfloat16)
    return (block_out, feature_grad, up_grad, down_grad, kernel_grad)


def solution(mesh):
    torus = Mesh(mesh.devices.reshape(SIZES), AXES)
    strips = P(DP, "rows", None, None)
    return jax.shard_map(
        on_device,
        mesh=torus,
        in_specs=(strips, P(DP), P(), P(DP, None), P(DP, None), strips),
        out_specs=(strips, strips, P(DP, None), P(DP, None), P()),
        check_vma=False,
    )
```

```python
import jax
import jax.numpy as jnp
from jax import lax
from jax.sharding import Mesh
from jax.sharding import PartitionSpec as P

INV_ROOT_TWO = 0.7071067811865476
INV_ROOT_TAU = 0.3989422804014327
EPSILON = 1e-06

AXES = ("y", "z", "xl", "c", "rows")
SIZES = (4, 8, 2, 2, 2)
DP = AXES[:4]
SIZE = dict(zip(AXES, SIZES))


def ring_scatter(x, axis, wire):
    n = SIZE[axis]
    me = lax.axis_index(axis)
    dim = AXES.index(axis)

    def block(j):
        return lax.dynamic_slice_in_dim(x, j % n, 1, dim)

    if n == 2:
        got = lax.ppermute(block(me + 1).astype(wire), axis, [(0, 1), (1, 0)])
        return block(me) + got.astype(jnp.float32)
    half = x.shape[-1] // 2
    acc_r = block(me - 1)[..., :half]
    acc_l = block(me + 1)[..., half:]
    for s in range(1, n):
        got_r = lax.ppermute(acc_r.astype(wire), axis, [(i, (i + 1) % n) for i in range(n)])
        got_l = lax.ppermute(acc_l.astype(wire), axis, [(i, (i - 1) % n) for i in range(n)])
        j_r, j_l = (me - s - 1, me + s + 1) if s < n - 1 else (me, me)
        acc_r = got_r.astype(jnp.float32) + block(j_r)[..., :half]
        acc_l = got_l.astype(jnp.float32) + block(j_l)[..., half:]
    return jnp.concatenate([acc_r, acc_l], axis=-1)


def ring_gather_rows(x, axis):
    n = SIZE[axis]
    me = lax.axis_index(axis)
    m = x.shape[0]
    out = jnp.zeros((n * m,) + x.shape[1:], x.dtype)
    out = lax.dynamic_update_slice_in_dim(out, x, me * m, 0)
    right = n // 2
    left = n - 1 - right
    cur = x
    for s in range(1, right + 1):
        cur = lax.ppermute(cur, axis, [(i, (i + 1) % n) for i in range(n)])
        out = lax.dynamic_update_slice_in_dim(out, cur, ((me - s) % n) * m, 0)
    cur = x
    for s in range(1, left + 1):
        cur = lax.ppermute(cur, axis, [(i, (i - 1) % n) for i in range(n)])
        out = lax.dynamic_update_slice_in_dim(out, cur, ((me + s) % n) * m, 0)
    return out


def gather_weight(shard):
    for axis in ("c", "xl", "y", "z"):
        shard = ring_gather_rows(shard, axis)
    shard = shard.reshape(SIZE["z"], SIZE["y"], -1, shard.shape[1]).transpose(1, 0, 2, 3)
    return shard.reshape(-1, shard.shape[3])


def reduce_weight_grad(term, order):
    rows = term.shape[0] // 128
    view = term.reshape(*SIZES[:4], 1, rows, term.shape[1])
    for axis in order:
        view = ring_scatter(view, axis, jnp.bfloat16)
    tiles = view.reshape(rows, term.shape[1])
    return tiles + lax.ppermute(tiles, "rows", [(0, 1), (1, 0)])


def butterfly_sum(x):
    for axis, n in zip(AXES, SIZES):
        d = 1
        while d < n:
            x = x + lax.ppermute(x, axis, [(i, i ^ d) for i in range(n)])
            d *= 2
    return x


def padded_2(block, sides, width):
    for axis, dim in sides:
        count = lax.axis_size(axis)
        forward = [(i, i + 1) for i in range(count - 1)]
        backward = [(target, source) for source, target in forward]
        low = lax.ppermute(
            lax.slice_in_dim(block, block.shape[dim] - width, None, axis=dim), axis, forward
        )
        high = lax.ppermute(lax.slice_in_dim(block, 0, width, axis=dim), axis, backward)
        block = jnp.concatenate([low, block, high], axis=dim)
    return block


def gelu_parts(pre_act):
    normal_cdf = 0.5 * (1.0 + lax.erf(pre_act * INV_ROOT_TWO))
    density = jnp.exp(-0.5 * pre_act * pre_act) * INV_ROOT_TAU
    return (pre_act * normal_cdf, normal_cdf + pre_act * density)


def depthwise(padded, kernel, out_rows, out_cols, flipped):
    span = kernel.shape[0]
    result = jnp.zeros(padded.shape[:-3] + (out_rows, out_cols, padded.shape[-1]), jnp.float32)
    for offset_row in range(span):
        for offset_col in range(span):
            start_row = span - 1 - offset_row if flipped else offset_row
            start_col = span - 1 - offset_col if flipped else offset_col
            result = (
                result
                + kernel[offset_row, offset_col]
                * padded[..., start_row : start_row + out_rows, start_col : start_col + out_cols, :]
            )
    return result


def kernel_terms(grad_conv, padded, span):
    reduce_axes = tuple(range(grad_conv.ndim - 1))
    rows_out = grad_conv.shape[-3]
    cols_out = grad_conv.shape[-2]
    kernel_rows = []
    for offset_row in range(span):
        kernel_row = []
        for offset_col in range(span):
            window = padded[
                ..., offset_row : offset_row + rows_out, offset_col : offset_col + cols_out, :
            ]
            kernel_row.append(jnp.sum(grad_conv * window, axis=reduce_axes))
        kernel_rows.append(jnp.stack(kernel_row))
    return jnp.stack(kernel_rows)


def layer_norm(convolved):
    centered = convolved - jnp.mean(convolved, axis=-1, keepdims=True)
    inv_std = lax.rsqrt(jnp.mean(centered * centered, axis=-1, keepdims=True) + EPSILON)
    return (centered * inv_std, inv_std)


def norm_backward(grad_norm, unit_norm, inv_std):
    first_mean = jnp.mean(grad_norm, axis=-1, keepdims=True)
    second_mean = jnp.mean(grad_norm * unit_norm, axis=-1, keepdims=True)
    return inv_std * (grad_norm - first_mean - unit_norm * second_mean)


def on_device(features, bucket, kernel, up_weight, down_weight, cotangent):
    images, strip_rows, canvas_cols, channels = features.shape
    rows_count = lax.axis_size("rows")
    row_index = lax.axis_index("rows")
    canvas_rows = strip_rows * rows_count
    area_cells = canvas_rows * canvas_cols // 2
    reach = kernel.shape[0] // 2
    grad_scale = 1.0 / (images * lax.axis_size(DP))
    heights = canvas_rows // 2 + bucket
    widths = jnp.minimum(canvas_cols, area_cells // heights)
    row_ids = row_index * strip_rows + lax.iota(jnp.int32, strip_rows)
    col_ids = lax.iota(jnp.int32, canvas_cols)
    inside = (row_ids[None, :, None] < heights[:, None, None]) & (
        col_ids[None, None, :] < widths[:, None, None]
    )
    inside_cells = inside[..., None]
    masked = jnp.where(inside_cells, features, jnp.zeros((), features.dtype))
    masked_cot = jnp.where(inside_cells, cotangent, jnp.zeros((), cotangent.dtype))
    up_full = gather_weight(up_weight)
    down_full = gather_weight(down_weight)
    rimmed = padded_2(masked, (("rows", 1),), reach)
    padded = jnp.pad(rimmed, ((0, 0), (0, 0), (reach, reach), (0, 0)))
    convolved = jnp.where(
        inside_cells, depthwise(padded, kernel, strip_rows, canvas_cols, False), 0.0
    )
    unit_norm, inv_std = layer_norm(convolved)
    normed = unit_norm.astype(jnp.bfloat16)
    tokens = normed.reshape(images * strip_rows * canvas_cols, channels)
    cot_rows = masked_cot.reshape(images * strip_rows * canvas_cols, channels)

    pre_act = jnp.dot(tokens, up_full, preferred_element_type=jnp.float32)
    hidden, derivative = gelu_parts(pre_act)
    activation = hidden.astype(jnp.bfloat16)
    down_term = lax.dot_general(
        activation, cot_rows, (((0,), (0,)), ((), ())), preferred_element_type=jnp.float32
    )
    down_grad = reduce_weight_grad(down_term * grad_scale, ("c", "y", "z", "xl"))
    branch = jnp.dot(activation, down_full, preferred_element_type=jnp.float32)
    grad_act = lax.dot_general(
        cot_rows, down_full, (((1,), (1,)), ((), ())), preferred_element_type=jnp.float32
    )
    grad_pre = (grad_act * derivative).astype(jnp.bfloat16)
    up_term = lax.dot_general(
        tokens, grad_pre, (((0,), (0,)), ((), ())), preferred_element_type=jnp.float32
    )
    up_grad = reduce_weight_grad(up_term * grad_scale, ("c", "z", "y", "xl"))
    grad_rows = lax.dot_general(
        grad_pre, up_full, (((1,), (1,)), ((), ())), preferred_element_type=jnp.float32
    )

    branch = branch.reshape(features.shape)
    grad_norm = grad_rows.reshape(features.shape)
    block_out = (masked + branch).astype(jnp.bfloat16)
    grad_conv = jnp.where(inside_cells, norm_backward(grad_norm, unit_norm, inv_std), 0.0)
    kernel_grad = butterfly_sum(kernel_terms(grad_conv, padded, kernel.shape[0]) * grad_scale)
    grad_rimmed = padded_2(grad_conv.astype(jnp.bfloat16), (("rows", 1),), reach).astype(
        grad_conv.dtype
    )
    grad_padded = jnp.pad(grad_rimmed, ((0, 0), (0, 0), (reach, reach), (0, 0)))
    feature_grad = jnp.where(
        inside_cells,
        masked_cot + depthwise(grad_padded, kernel, strip_rows, canvas_cols, True),
        0.0,
    ).astype(jnp.bfloat16)
    return (block_out, feature_grad, up_grad, down_grad, kernel_grad)


def solution(mesh):
    torus = Mesh(mesh.devices.reshape(SIZES), AXES)
    strips = P(DP, "rows", None, None)
    return jax.shard_map(
        on_device,
        mesh=torus,
        in_specs=(strips, P(DP), P(), P(DP, None), P(DP, None), strips),
        out_specs=(strips, strips, P(DP, None), P(DP, None), P()),
        check_vma=False,
    )
```

```python
import jax
import jax.numpy as jnp
from jax import lax
from jax.sharding import Mesh
from jax.sharding import PartitionSpec as P

INV_ROOT_TWO = 0.7071067811865476
INV_ROOT_TAU = 0.3989422804014327
EPSILON = 1e-06

AXES = ("y", "z", "xl", "c", "rows")
SIZES = (4, 8, 2, 2, 2)
DP = AXES[:4]
SIZE = dict(zip(AXES, SIZES))


def ring_scatter(x, axis, wire):
    n = SIZE[axis]
    me = lax.axis_index(axis)
    dim = AXES.index(axis)
    d = 1
    while d < n:
        shape = list(x.shape)
        shape[dim : dim + 1] = [shape[dim] // 2, 2]
        pairs = x.reshape(shape)
        bit = (me // d) % 2
        keep = lax.dynamic_index_in_dim(pairs, bit, dim + 1, keepdims=False)
        send = lax.dynamic_index_in_dim(pairs, 1 - bit, dim + 1, keepdims=False)
        got = lax.ppermute(send.astype(wire), axis, [(i, i ^ d) for i in range(n)])
        x = keep + got.astype(jnp.float32)
        d *= 2
    return x


def ring_gather_rows(x, axis):
    n = SIZE[axis]
    me = lax.axis_index(axis)
    m = x.shape[0]
    out = jnp.zeros((n * m,) + x.shape[1:], x.dtype)
    out = lax.dynamic_update_slice_in_dim(out, x, me * m, 0)
    right = n // 2
    left = n - 1 - right
    cur = x
    for s in range(1, right + 1):
        cur = lax.ppermute(cur, axis, [(i, (i + 1) % n) for i in range(n)])
        out = lax.dynamic_update_slice_in_dim(out, cur, ((me - s) % n) * m, 0)
    cur = x
    for s in range(1, left + 1):
        cur = lax.ppermute(cur, axis, [(i, (i - 1) % n) for i in range(n)])
        out = lax.dynamic_update_slice_in_dim(out, cur, ((me + s) % n) * m, 0)
    return out


def gather_weight(shard):
    for axis in ("c", "xl", "y", "z"):
        shard = ring_gather_rows(shard, axis)
    shard = shard.reshape(SIZE["z"], SIZE["y"], -1, shard.shape[1]).transpose(1, 0, 2, 3)
    return shard.reshape(-1, shard.shape[3])


def reduce_weight_grad(term, order):
    rows = term.shape[0] // 128
    view = term.reshape(*SIZES[:4], 1, rows, term.shape[1])
    for axis in order:
        view = ring_scatter(view, axis, jnp.bfloat16)
    tiles = view.reshape(rows, term.shape[1])
    return tiles + lax.ppermute(tiles, "rows", [(0, 1), (1, 0)])


def butterfly_sum(x):
    for axis, n in zip(AXES, SIZES):
        d = 1
        while d < n:
            x = x + lax.ppermute(x, axis, [(i, i ^ d) for i in range(n)])
            d *= 2
    return x


def padded_2(block, sides, width):
    for axis, dim in sides:
        count = lax.axis_size(axis)
        forward = [(i, i + 1) for i in range(count - 1)]
        backward = [(target, source) for source, target in forward]
        low = lax.ppermute(
            lax.slice_in_dim(block, block.shape[dim] - width, None, axis=dim), axis, forward
        )
        high = lax.ppermute(lax.slice_in_dim(block, 0, width, axis=dim), axis, backward)
        block = jnp.concatenate([low, block, high], axis=dim)
    return block


def gelu_parts(pre_act):
    normal_cdf = 0.5 * (1.0 + lax.erf(pre_act * INV_ROOT_TWO))
    density = jnp.exp(-0.5 * pre_act * pre_act) * INV_ROOT_TAU
    return (pre_act * normal_cdf, normal_cdf + pre_act * density)


def depthwise(padded, kernel, out_rows, out_cols, flipped):
    span = kernel.shape[0]
    result = jnp.zeros(padded.shape[:-3] + (out_rows, out_cols, padded.shape[-1]), jnp.float32)
    for offset_row in range(span):
        for offset_col in range(span):
            start_row = span - 1 - offset_row if flipped else offset_row
            start_col = span - 1 - offset_col if flipped else offset_col
            result = (
                result
                + kernel[offset_row, offset_col]
                * padded[..., start_row : start_row + out_rows, start_col : start_col + out_cols, :]
            )
    return result


def kernel_terms(grad_conv, padded, span):
    reduce_axes = tuple(range(grad_conv.ndim - 1))
    rows_out = grad_conv.shape[-3]
    cols_out = grad_conv.shape[-2]
    kernel_rows = []
    for offset_row in range(span):
        kernel_row = []
        for offset_col in range(span):
            window = padded[
                ..., offset_row : offset_row + rows_out, offset_col : offset_col + cols_out, :
            ]
            kernel_row.append(jnp.sum(grad_conv * window, axis=reduce_axes))
        kernel_rows.append(jnp.stack(kernel_row))
    return jnp.stack(kernel_rows)


def layer_norm(convolved):
    centered = convolved - jnp.mean(convolved, axis=-1, keepdims=True)
    inv_std = lax.rsqrt(jnp.mean(centered * centered, axis=-1, keepdims=True) + EPSILON)
    return (centered * inv_std, inv_std)


def norm_backward(grad_norm, unit_norm, inv_std):
    first_mean = jnp.mean(grad_norm, axis=-1, keepdims=True)
    second_mean = jnp.mean(grad_norm * unit_norm, axis=-1, keepdims=True)
    return inv_std * (grad_norm - first_mean - unit_norm * second_mean)


def on_device(features, bucket, kernel, up_weight, down_weight, cotangent):
    images, strip_rows, canvas_cols, channels = features.shape
    rows_count = lax.axis_size("rows")
    row_index = lax.axis_index("rows")
    canvas_rows = strip_rows * rows_count
    area_cells = canvas_rows * canvas_cols // 2
    reach = kernel.shape[0] // 2
    grad_scale = 1.0 / (images * lax.axis_size(DP))
    heights = canvas_rows // 2 + bucket
    widths = jnp.minimum(canvas_cols, area_cells // heights)
    row_ids = row_index * strip_rows + lax.iota(jnp.int32, strip_rows)
    col_ids = lax.iota(jnp.int32, canvas_cols)
    inside = (row_ids[None, :, None] < heights[:, None, None]) & (
        col_ids[None, None, :] < widths[:, None, None]
    )
    inside_cells = inside[..., None]
    masked = jnp.where(inside_cells, features, jnp.zeros((), features.dtype))
    masked_cot = jnp.where(inside_cells, cotangent, jnp.zeros((), cotangent.dtype))
    up_full = gather_weight(up_weight)
    down_full = gather_weight(down_weight)
    rimmed = padded_2(masked, (("rows", 1),), reach)
    padded = jnp.pad(rimmed, ((0, 0), (0, 0), (reach, reach), (0, 0)))
    convolved = jnp.where(
        inside_cells, depthwise(padded, kernel, strip_rows, canvas_cols, False), 0.0
    )
    unit_norm, inv_std = layer_norm(convolved)
    normed = unit_norm.astype(jnp.bfloat16)
    tokens = normed.reshape(images * strip_rows * canvas_cols, channels)
    cot_rows = masked_cot.reshape(images * strip_rows * canvas_cols, channels)

    pre_act = jnp.dot(tokens, up_full, preferred_element_type=jnp.float32)
    hidden, derivative = gelu_parts(pre_act)
    activation = hidden.astype(jnp.bfloat16)
    down_term = lax.dot_general(
        activation, cot_rows, (((0,), (0,)), ((), ())), preferred_element_type=jnp.float32
    )
    down_grad = reduce_weight_grad(down_term * grad_scale, ("c", "y", "z", "xl"))
    branch = jnp.dot(activation, down_full, preferred_element_type=jnp.float32)
    grad_act = lax.dot_general(
        cot_rows, down_full, (((1,), (1,)), ((), ())), preferred_element_type=jnp.float32
    )
    grad_pre = (grad_act * derivative).astype(jnp.bfloat16)
    up_term = lax.dot_general(
        tokens, grad_pre, (((0,), (0,)), ((), ())), preferred_element_type=jnp.float32
    )
    up_grad = reduce_weight_grad(up_term * grad_scale, ("c", "z", "y", "xl"))
    grad_rows = lax.dot_general(
        grad_pre, up_full, (((1,), (1,)), ((), ())), preferred_element_type=jnp.float32
    )

    branch = branch.reshape(features.shape)
    grad_norm = grad_rows.reshape(features.shape)
    block_out = (masked + branch).astype(jnp.bfloat16)
    grad_conv = jnp.where(inside_cells, norm_backward(grad_norm, unit_norm, inv_std), 0.0)
    kernel_grad = butterfly_sum(kernel_terms(grad_conv, padded, kernel.shape[0]) * grad_scale)
    grad_rimmed = padded_2(grad_conv.astype(jnp.bfloat16), (("rows", 1),), reach).astype(
        grad_conv.dtype
    )
    grad_padded = jnp.pad(grad_rimmed, ((0, 0), (0, 0), (reach, reach), (0, 0)))
    feature_grad = jnp.where(
        inside_cells,
        masked_cot + depthwise(grad_padded, kernel, strip_rows, canvas_cols, True),
        0.0,
    ).astype(jnp.bfloat16)
    return (block_out, feature_grad, up_grad, down_grad, kernel_grad)


def solution(mesh):
    torus = Mesh(mesh.devices.reshape(SIZES), AXES)
    strips = P(DP, "rows", None, None)
    return jax.shard_map(
        on_device,
        mesh=torus,
        in_specs=(strips, P(DP), P(), P(DP, None), P(DP, None), strips),
        out_specs=(strips, strips, P(DP, None), P(DP, None), P()),
        check_vma=False,
    )
```

```python
import jax
import jax.numpy as jnp
from jax import lax
from jax.sharding import Mesh
from jax.sharding import PartitionSpec as P

INV_ROOT_TWO = 0.7071067811865476
INV_ROOT_TAU = 0.3989422804014327
EPSILON = 1e-06

AXES = ("y", "z", "xl", "c", "rows")
SIZES = (4, 8, 2, 2, 2)
DP = AXES[:4]
SIZE = dict(zip(AXES, SIZES))


def ring_scatter(x, axis, wire):
    n = SIZE[axis]
    me = lax.axis_index(axis)
    dim = AXES.index(axis)
    d = 1
    while d < n:
        shape = list(x.shape)
        shape[dim : dim + 1] = [shape[dim] // 2, 2]
        pairs = x.reshape(shape)
        bit = (me // d) % 2
        keep = lax.dynamic_index_in_dim(pairs, bit, dim + 1, keepdims=False)
        send = lax.dynamic_index_in_dim(pairs, 1 - bit, dim + 1, keepdims=False)
        got = lax.ppermute(send.astype(wire), axis, [(i, i ^ d) for i in range(n)])
        x = keep + got.astype(jnp.float32)
        d *= 2
    return x


def ring_gather_rows(x, axis):
    n = SIZE[axis]
    me = lax.axis_index(axis)
    m = x.shape[0]
    out = jnp.zeros((n * m,) + x.shape[1:], x.dtype)
    out = lax.dynamic_update_slice_in_dim(out, x, me * m, 0)
    right = n // 2
    left = n - 1 - right
    cur = x
    for s in range(1, right + 1):
        cur = lax.ppermute(cur, axis, [(i, (i + 1) % n) for i in range(n)])
        out = lax.dynamic_update_slice_in_dim(out, cur, ((me - s) % n) * m, 0)
    cur = x
    for s in range(1, left + 1):
        cur = lax.ppermute(cur, axis, [(i, (i - 1) % n) for i in range(n)])
        out = lax.dynamic_update_slice_in_dim(out, cur, ((me + s) % n) * m, 0)
    return out


def gather_weight(shard):
    order = ("xl", "y", "z", "c")
    for axis in order:
        shard = ring_gather_rows(shard, axis)
    gathered = tuple(reversed(order))
    shard = shard.reshape(*(SIZE[a] for a in gathered), -1, shard.shape[1])
    shard = shard.transpose([gathered.index(a) for a in DP] + [4, 5])
    return shard.reshape(-1, shard.shape[5])


def reduce_weight_grad(term, order):
    rows = term.shape[0] // 128
    view = term.reshape(*SIZES[:4], 1, rows, term.shape[1])
    for axis in order:
        view = ring_scatter(view, axis, jnp.bfloat16)
    tiles = view.reshape(rows, term.shape[1])
    return tiles + lax.ppermute(tiles, "rows", [(0, 1), (1, 0)])


def butterfly_sum(x):
    for axis, n in zip(AXES, SIZES):
        d = 1
        while d < n:
            x = x + lax.ppermute(x, axis, [(i, i ^ d) for i in range(n)])
            d *= 2
    return x


def padded_2(block, sides, width):
    for axis, dim in sides:
        count = lax.axis_size(axis)
        forward = [(i, i + 1) for i in range(count - 1)]
        backward = [(target, source) for source, target in forward]
        low = lax.ppermute(
            lax.slice_in_dim(block, block.shape[dim] - width, None, axis=dim), axis, forward
        )
        high = lax.ppermute(lax.slice_in_dim(block, 0, width, axis=dim), axis, backward)
        block = jnp.concatenate([low, block, high], axis=dim)
    return block


def gelu_parts(pre_act):
    normal_cdf = 0.5 * (1.0 + lax.erf(pre_act * INV_ROOT_TWO))
    density = jnp.exp(-0.5 * pre_act * pre_act) * INV_ROOT_TAU
    return (pre_act * normal_cdf, normal_cdf + pre_act * density)


def depthwise(padded, kernel, out_rows, out_cols, flipped):
    span = kernel.shape[0]
    result = jnp.zeros(padded.shape[:-3] + (out_rows, out_cols, padded.shape[-1]), jnp.float32)
    for offset_row in range(span):
        for offset_col in range(span):
            start_row = span - 1 - offset_row if flipped else offset_row
            start_col = span - 1 - offset_col if flipped else offset_col
            result = (
                result
                + kernel[offset_row, offset_col]
                * padded[..., start_row : start_row + out_rows, start_col : start_col + out_cols, :]
            )
    return result


def kernel_terms(grad_conv, padded, span):
    reduce_axes = tuple(range(grad_conv.ndim - 1))
    rows_out = grad_conv.shape[-3]
    cols_out = grad_conv.shape[-2]
    kernel_rows = []
    for offset_row in range(span):
        kernel_row = []
        for offset_col in range(span):
            window = padded[
                ..., offset_row : offset_row + rows_out, offset_col : offset_col + cols_out, :
            ]
            kernel_row.append(jnp.sum(grad_conv * window, axis=reduce_axes))
        kernel_rows.append(jnp.stack(kernel_row))
    return jnp.stack(kernel_rows)


def layer_norm(convolved):
    centered = convolved - jnp.mean(convolved, axis=-1, keepdims=True)
    inv_std = lax.rsqrt(jnp.mean(centered * centered, axis=-1, keepdims=True) + EPSILON)
    return (centered * inv_std, inv_std)


def norm_backward(grad_norm, unit_norm, inv_std):
    first_mean = jnp.mean(grad_norm, axis=-1, keepdims=True)
    second_mean = jnp.mean(grad_norm * unit_norm, axis=-1, keepdims=True)
    return inv_std * (grad_norm - first_mean - unit_norm * second_mean)


def on_device(features, bucket, kernel, up_weight, down_weight, cotangent):
    images, strip_rows, canvas_cols, channels = features.shape
    rows_count = lax.axis_size("rows")
    row_index = lax.axis_index("rows")
    canvas_rows = strip_rows * rows_count
    area_cells = canvas_rows * canvas_cols // 2
    reach = kernel.shape[0] // 2
    grad_scale = 1.0 / (images * lax.axis_size(DP))
    heights = canvas_rows // 2 + bucket
    widths = jnp.minimum(canvas_cols, area_cells // heights)
    row_ids = row_index * strip_rows + lax.iota(jnp.int32, strip_rows)
    col_ids = lax.iota(jnp.int32, canvas_cols)
    inside = (row_ids[None, :, None] < heights[:, None, None]) & (
        col_ids[None, None, :] < widths[:, None, None]
    )
    inside_cells = inside[..., None]
    masked = jnp.where(inside_cells, features, jnp.zeros((), features.dtype))
    masked_cot = jnp.where(inside_cells, cotangent, jnp.zeros((), cotangent.dtype))
    up_full = gather_weight(up_weight)
    down_full = gather_weight(down_weight)
    rimmed = padded_2(masked, (("rows", 1),), reach)
    padded = jnp.pad(rimmed, ((0, 0), (0, 0), (reach, reach), (0, 0)))
    convolved = jnp.where(
        inside_cells, depthwise(padded, kernel, strip_rows, canvas_cols, False), 0.0
    )
    unit_norm, inv_std = layer_norm(convolved)
    normed = unit_norm.astype(jnp.bfloat16)
    tokens = normed.reshape(images * strip_rows * canvas_cols, channels)
    cot_rows = masked_cot.reshape(images * strip_rows * canvas_cols, channels)

    pre_act = jnp.dot(tokens, up_full, preferred_element_type=jnp.float32)
    hidden, derivative = gelu_parts(pre_act)
    activation = hidden.astype(jnp.bfloat16)
    down_term = lax.dot_general(
        activation, cot_rows, (((0,), (0,)), ((), ())), preferred_element_type=jnp.float32
    )
    down_grad = reduce_weight_grad(down_term * grad_scale, ("c", "y", "z", "xl"))
    branch = jnp.dot(activation, down_full, preferred_element_type=jnp.float32)
    grad_act = lax.dot_general(
        cot_rows, down_full, (((1,), (1,)), ((), ())), preferred_element_type=jnp.float32
    )
    grad_pre = (grad_act * derivative).astype(jnp.bfloat16)
    up_term = lax.dot_general(
        tokens, grad_pre, (((0,), (0,)), ((), ())), preferred_element_type=jnp.float32
    )
    up_grad = reduce_weight_grad(up_term * grad_scale, ("c", "z", "y", "xl"))
    grad_rows = lax.dot_general(
        grad_pre, up_full, (((1,), (1,)), ((), ())), preferred_element_type=jnp.float32
    )

    branch = branch.reshape(features.shape)
    grad_norm = grad_rows.reshape(features.shape)
    block_out = (masked + branch).astype(jnp.bfloat16)
    grad_conv = jnp.where(inside_cells, norm_backward(grad_norm, unit_norm, inv_std), 0.0)
    kernel_grad = butterfly_sum(kernel_terms(grad_conv, padded, kernel.shape[0]) * grad_scale)
    grad_rimmed = padded_2(grad_conv.astype(jnp.bfloat16), (("rows", 1),), reach).astype(
        grad_conv.dtype
    )
    grad_padded = jnp.pad(grad_rimmed, ((0, 0), (0, 0), (reach, reach), (0, 0)))
    feature_grad = jnp.where(
        inside_cells,
        masked_cot + depthwise(grad_padded, kernel, strip_rows, canvas_cols, True),
        0.0,
    ).astype(jnp.bfloat16)
    return (block_out, feature_grad, up_grad, down_grad, kernel_grad)


def solution(mesh):
    torus = Mesh(mesh.devices.reshape(SIZES), AXES)
    strips = P(DP, "rows", None, None)
    return jax.shard_map(
        on_device,
        mesh=torus,
        in_specs=(strips, P(DP), P(), P(DP, None), P(DP, None), strips),
        out_specs=(strips, strips, P(DP, None), P(DP, None), P()),
        check_vma=False,
    )
```

```python
import jax
import jax.numpy as jnp
from jax import lax
from jax.sharding import Mesh
from jax.sharding import PartitionSpec as P

INV_ROOT_TWO = 0.7071067811865476
INV_ROOT_TAU = 0.3989422804014327
EPSILON = 1e-06

AXES = ("y", "z", "xl", "c", "rows")
SIZES = (4, 8, 2, 2, 2)
DP = AXES[:4]
SIZE = dict(zip(AXES, SIZES))


def ring_scatter(x, axis, wire, dim):
    n = SIZE[axis]
    me = lax.axis_index(axis)
    d = 1
    while d < n:
        shape = list(x.shape)
        shape[dim : dim + 1] = [shape[dim] // 2, 2]
        pairs = x.reshape(shape)
        bit = (me // d) % 2
        keep = lax.dynamic_index_in_dim(pairs, bit, dim + 1, keepdims=False)
        send = lax.dynamic_index_in_dim(pairs, 1 - bit, dim + 1, keepdims=False)
        got = lax.ppermute(send.astype(wire), axis, [(i, i ^ d) for i in range(n)])
        x = keep + got.astype(jnp.float32)
        d *= 2
    return x


def ring_gather_rows(x, axis):
    n = SIZE[axis]
    me = lax.axis_index(axis)
    m = x.shape[0]
    out = jnp.zeros((n * m,) + x.shape[1:], x.dtype)
    out = lax.dynamic_update_slice_in_dim(out, x, me * m, 0)
    right = n // 2
    left = n - 1 - right
    cur = x
    for s in range(1, right + 1):
        cur = lax.ppermute(cur, axis, [(i, (i + 1) % n) for i in range(n)])
        out = lax.dynamic_update_slice_in_dim(out, cur, ((me - s) % n) * m, 0)
    cur = x
    for s in range(1, left + 1):
        cur = lax.ppermute(cur, axis, [(i, (i - 1) % n) for i in range(n)])
        out = lax.dynamic_update_slice_in_dim(out, cur, ((me + s) % n) * m, 0)
    return out


GATHERED = ("c", "z", "y", "xl")


def to_gathered(x):
    lead = x.shape[:-1]
    x = x.reshape(*lead, *SIZES[:4], -1)
    k = len(lead)
    x = jnp.transpose(x, [*range(k), *(k + DP.index(a) for a in GATHERED), k + 4])
    return x.reshape(*lead, -1)


def from_gathered(x):
    lead = x.shape[:-1]
    x = x.reshape(*lead, *(SIZE[a] for a in GATHERED), -1)
    k = len(lead)
    x = jnp.transpose(x, [*range(k), *(k + GATHERED.index(a) for a in DP), k + 4])
    return x.reshape(*lead, -1)


def gather_weight(shard):
    for axis in reversed(GATHERED):
        shard = ring_gather_rows(shard, axis)
    return shard


def reduce_weight_grad(term, order):
    rows = term.shape[0] // 128
    view = term.reshape(*(SIZE[a] for a in GATHERED), 1, rows, term.shape[1])
    for axis in order:
        view = ring_scatter(view, axis, jnp.bfloat16, GATHERED.index(axis))
    tiles = view.reshape(rows, term.shape[1])
    return tiles + lax.ppermute(tiles, "rows", [(0, 1), (1, 0)])


def butterfly_sum(x):
    for axis, n in zip(AXES, SIZES):
        d = 1
        while d < n:
            x = x + lax.ppermute(x, axis, [(i, i ^ d) for i in range(n)])
            d *= 2
    return x


def padded_2(block, sides, width):
    for axis, dim in sides:
        count = lax.axis_size(axis)
        forward = [(i, i + 1) for i in range(count - 1)]
        backward = [(target, source) for source, target in forward]
        low = lax.ppermute(
            lax.slice_in_dim(block, block.shape[dim] - width, None, axis=dim), axis, forward
        )
        high = lax.ppermute(lax.slice_in_dim(block, 0, width, axis=dim), axis, backward)
        block = jnp.concatenate([low, block, high], axis=dim)
    return block


def gelu_parts(pre_act):
    normal_cdf = 0.5 * (1.0 + lax.erf(pre_act * INV_ROOT_TWO))
    density = jnp.exp(-0.5 * pre_act * pre_act) * INV_ROOT_TAU
    return (pre_act * normal_cdf, normal_cdf + pre_act * density)


def depthwise(padded, kernel, out_rows, out_cols, flipped):
    span = kernel.shape[0]
    result = jnp.zeros(padded.shape[:-3] + (out_rows, out_cols, padded.shape[-1]), jnp.float32)
    for offset_row in range(span):
        for offset_col in range(span):
            start_row = span - 1 - offset_row if flipped else offset_row
            start_col = span - 1 - offset_col if flipped else offset_col
            result = (
                result
                + kernel[offset_row, offset_col]
                * padded[..., start_row : start_row + out_rows, start_col : start_col + out_cols, :]
            )
    return result


def kernel_terms(grad_conv, padded, span):
    reduce_axes = tuple(range(grad_conv.ndim - 1))
    rows_out = grad_conv.shape[-3]
    cols_out = grad_conv.shape[-2]
    kernel_rows = []
    for offset_row in range(span):
        kernel_row = []
        for offset_col in range(span):
            window = padded[
                ..., offset_row : offset_row + rows_out, offset_col : offset_col + cols_out, :
            ]
            kernel_row.append(jnp.sum(grad_conv * window, axis=reduce_axes))
        kernel_rows.append(jnp.stack(kernel_row))
    return jnp.stack(kernel_rows)


def layer_norm(convolved):
    centered = convolved - jnp.mean(convolved, axis=-1, keepdims=True)
    inv_std = lax.rsqrt(jnp.mean(centered * centered, axis=-1, keepdims=True) + EPSILON)
    return (centered * inv_std, inv_std)


def norm_backward(grad_norm, unit_norm, inv_std):
    first_mean = jnp.mean(grad_norm, axis=-1, keepdims=True)
    second_mean = jnp.mean(grad_norm * unit_norm, axis=-1, keepdims=True)
    return inv_std * (grad_norm - first_mean - unit_norm * second_mean)


def on_device(features, bucket, kernel, up_weight, down_weight, cotangent):
    images, strip_rows, canvas_cols, channels = features.shape
    rows_count = lax.axis_size("rows")
    row_index = lax.axis_index("rows")
    canvas_rows = strip_rows * rows_count
    area_cells = canvas_rows * canvas_cols // 2
    reach = kernel.shape[0] // 2
    grad_scale = 1.0 / (images * lax.axis_size(DP))
    heights = canvas_rows // 2 + bucket
    widths = jnp.minimum(canvas_cols, area_cells // heights)
    row_ids = row_index * strip_rows + lax.iota(jnp.int32, strip_rows)
    col_ids = lax.iota(jnp.int32, canvas_cols)
    inside = (row_ids[None, :, None] < heights[:, None, None]) & (
        col_ids[None, None, :] < widths[:, None, None]
    )
    inside_cells = inside[..., None]
    masked = jnp.where(inside_cells, features, jnp.zeros((), features.dtype))
    masked_cot = jnp.where(inside_cells, cotangent, jnp.zeros((), cotangent.dtype))
    up_full = gather_weight(to_gathered(up_weight))
    down_full = gather_weight(down_weight)
    rimmed = padded_2(masked, (("rows", 1),), reach)
    padded = jnp.pad(rimmed, ((0, 0), (0, 0), (reach, reach), (0, 0)))
    convolved = jnp.where(
        inside_cells, depthwise(padded, kernel, strip_rows, canvas_cols, False), 0.0
    )
    unit_norm, inv_std = layer_norm(convolved)
    normed = unit_norm.astype(jnp.bfloat16)
    tokens = normed.reshape(images * strip_rows * canvas_cols, channels)
    tokens_g = to_gathered(tokens)
    cot_rows = masked_cot.reshape(images * strip_rows * canvas_cols, channels)

    pre_act = jnp.dot(tokens_g, up_full, preferred_element_type=jnp.float32)
    hidden, derivative = gelu_parts(pre_act)
    activation = hidden.astype(jnp.bfloat16)
    down_term = lax.dot_general(
        activation, cot_rows, (((0,), (0,)), ((), ())), preferred_element_type=jnp.float32
    )
    down_grad = reduce_weight_grad(down_term * grad_scale, ("c", "y", "z", "xl"))
    branch = jnp.dot(activation, down_full, preferred_element_type=jnp.float32)
    grad_act = lax.dot_general(
        cot_rows, down_full, (((1,), (1,)), ((), ())), preferred_element_type=jnp.float32
    )
    grad_pre = (grad_act * derivative).astype(jnp.bfloat16)
    up_term = lax.dot_general(
        tokens_g, grad_pre, (((0,), (0,)), ((), ())), preferred_element_type=jnp.float32
    )
    up_grad = from_gathered(reduce_weight_grad(up_term * grad_scale, ("c", "z", "y", "xl")))
    grad_rows = lax.dot_general(
        grad_pre, up_full, (((1,), (1,)), ((), ())), preferred_element_type=jnp.float32
    )

    branch = branch.reshape(features.shape)
    grad_norm = from_gathered(grad_rows).reshape(features.shape)
    block_out = (masked + branch).astype(jnp.bfloat16)
    grad_conv = jnp.where(inside_cells, norm_backward(grad_norm, unit_norm, inv_std), 0.0)
    kernel_grad = butterfly_sum(kernel_terms(grad_conv, padded, kernel.shape[0]) * grad_scale)
    grad_rimmed = padded_2(grad_conv.astype(jnp.bfloat16), (("rows", 1),), reach).astype(
        grad_conv.dtype
    )
    grad_padded = jnp.pad(grad_rimmed, ((0, 0), (0, 0), (reach, reach), (0, 0)))
    feature_grad = jnp.where(
        inside_cells,
        masked_cot + depthwise(grad_padded, kernel, strip_rows, canvas_cols, True),
        0.0,
    ).astype(jnp.bfloat16)
    return (block_out, feature_grad, up_grad, down_grad, kernel_grad)


def solution(mesh):
    torus = Mesh(mesh.devices.reshape(SIZES), AXES)
    strips = P(DP, "rows", None, None)
    return jax.shard_map(
        on_device,
        mesh=torus,
        in_specs=(strips, P(DP), P(), P(DP, None), P(DP, None), strips),
        out_specs=(strips, strips, P(DP, None), P(DP, None), P()),
        check_vma=False,
    )
```

```python
import jax
import jax.numpy as jnp
from jax import lax
from jax.sharding import Mesh
from jax.sharding import PartitionSpec as P

INV_ROOT_TWO = 0.7071067811865476
INV_ROOT_TAU = 0.3989422804014327
EPSILON = 1e-06

AXES = ("y", "z", "xl", "c", "rows")
SIZES = (4, 8, 2, 2, 2)
DP = AXES[:4]
SIZE = dict(zip(AXES, SIZES))


def ring_scatter(x, axis, wire):
    n = SIZE[axis]
    me = lax.axis_index(axis)
    dim = AXES.index(axis)
    d = 1
    while d < n:
        shape = list(x.shape)
        shape[dim : dim + 1] = [shape[dim] // 2, 2]
        pairs = x.reshape(shape)
        bit = (me // d) % 2
        keep = lax.dynamic_index_in_dim(pairs, bit, dim + 1, keepdims=False)
        send = lax.dynamic_index_in_dim(pairs, 1 - bit, dim + 1, keepdims=False)
        got = lax.ppermute(send.astype(wire), axis, [(i, i ^ d) for i in range(n)])
        x = keep + got.astype(jnp.float32)
        d *= 2
    return x


def ring_gather_rows(x, axis):
    n = SIZE[axis]
    me = lax.axis_index(axis)
    m = x.shape[0]
    out = jnp.zeros((n * m,) + x.shape[1:], x.dtype)
    out = lax.dynamic_update_slice_in_dim(out, x, me * m, 0)
    right = n // 2
    left = n - 1 - right
    cur = x
    for s in range(1, right + 1):
        cur = lax.ppermute(cur, axis, [(i, (i + 1) % n) for i in range(n)])
        out = lax.dynamic_update_slice_in_dim(out, cur, ((me - s) % n) * m, 0)
    cur = x
    for s in range(1, left + 1):
        cur = lax.ppermute(cur, axis, [(i, (i - 1) % n) for i in range(n)])
        out = lax.dynamic_update_slice_in_dim(out, cur, ((me + s) % n) * m, 0)
    return out


def gather_weight(shard):
    for axis in ("c", "xl", "y", "z"):
        shard = ring_gather_rows(shard, axis)
    shard = shard.reshape(SIZE["z"], SIZE["y"], -1, shard.shape[1]).transpose(1, 0, 2, 3)
    return shard.reshape(-1, shard.shape[3])


def reduce_weight_grad(term, order):
    rows = term.shape[1]
    view = term.reshape(*SIZES[:4], 1, rows, term.shape[2])
    for axis in order:
        view = ring_scatter(view, axis, jnp.bfloat16)
    tiles = view.reshape(rows, term.shape[2])
    return tiles + lax.ppermute(tiles, "rows", [(0, 1), (1, 0)])


def butterfly_sum(x):
    for axis, n in zip(AXES, SIZES):
        d = 1
        while d < n:
            x = x + lax.ppermute(x, axis, [(i, i ^ d) for i in range(n)])
            d *= 2
    return x


def padded_2(block, sides, width):
    for axis, dim in sides:
        count = lax.axis_size(axis)
        forward = [(i, i + 1) for i in range(count - 1)]
        backward = [(target, source) for source, target in forward]
        low = lax.ppermute(
            lax.slice_in_dim(block, block.shape[dim] - width, None, axis=dim), axis, forward
        )
        high = lax.ppermute(lax.slice_in_dim(block, 0, width, axis=dim), axis, backward)
        block = jnp.concatenate([low, block, high], axis=dim)
    return block


def gelu_parts(pre_act):
    normal_cdf = 0.5 * (1.0 + lax.erf(pre_act * INV_ROOT_TWO))
    density = jnp.exp(-0.5 * pre_act * pre_act) * INV_ROOT_TAU
    return (pre_act * normal_cdf, normal_cdf + pre_act * density)


def depthwise(padded, kernel, out_rows, out_cols, flipped):
    span = kernel.shape[0]
    result = jnp.zeros(padded.shape[:-3] + (out_rows, out_cols, padded.shape[-1]), jnp.float32)
    for offset_row in range(span):
        for offset_col in range(span):
            start_row = span - 1 - offset_row if flipped else offset_row
            start_col = span - 1 - offset_col if flipped else offset_col
            result = (
                result
                + kernel[offset_row, offset_col]
                * padded[..., start_row : start_row + out_rows, start_col : start_col + out_cols, :]
            )
    return result


def kernel_terms(grad_conv, padded, span):
    reduce_axes = tuple(range(grad_conv.ndim - 1))
    rows_out = grad_conv.shape[-3]
    cols_out = grad_conv.shape[-2]
    kernel_rows = []
    for offset_row in range(span):
        kernel_row = []
        for offset_col in range(span):
            window = padded[
                ..., offset_row : offset_row + rows_out, offset_col : offset_col + cols_out, :
            ]
            kernel_row.append(jnp.sum(grad_conv * window, axis=reduce_axes))
        kernel_rows.append(jnp.stack(kernel_row))
    return jnp.stack(kernel_rows)


def layer_norm(convolved):
    centered = convolved - jnp.mean(convolved, axis=-1, keepdims=True)
    inv_std = lax.rsqrt(jnp.mean(centered * centered, axis=-1, keepdims=True) + EPSILON)
    return (centered * inv_std, inv_std)


def norm_backward(grad_norm, unit_norm, inv_std):
    first_mean = jnp.mean(grad_norm, axis=-1, keepdims=True)
    second_mean = jnp.mean(grad_norm * unit_norm, axis=-1, keepdims=True)
    return inv_std * (grad_norm - first_mean - unit_norm * second_mean)


def on_device(features, bucket, kernel, up_weight, down_weight, cotangent):
    images, strip_rows, canvas_cols, channels = features.shape
    rows_count = lax.axis_size("rows")
    row_index = lax.axis_index("rows")
    canvas_rows = strip_rows * rows_count
    area_cells = canvas_rows * canvas_cols // 2
    reach = kernel.shape[0] // 2
    grad_scale = 1.0 / (images * lax.axis_size(DP))
    heights = canvas_rows // 2 + bucket
    widths = jnp.minimum(canvas_cols, area_cells // heights)
    row_ids = row_index * strip_rows + lax.iota(jnp.int32, strip_rows)
    col_ids = lax.iota(jnp.int32, canvas_cols)
    inside = (row_ids[None, :, None] < heights[:, None, None]) & (
        col_ids[None, None, :] < widths[:, None, None]
    )
    inside_cells = inside[..., None]
    masked = jnp.where(inside_cells, features, jnp.zeros((), features.dtype))
    masked_cot = jnp.where(inside_cells, cotangent, jnp.zeros((), cotangent.dtype))
    up_full = gather_weight(up_weight)
    down_full = gather_weight(down_weight)
    rimmed = padded_2(masked, (("rows", 1),), reach)
    padded = jnp.pad(rimmed, ((0, 0), (0, 0), (reach, reach), (0, 0)))
    convolved = jnp.where(
        inside_cells, depthwise(padded, kernel, strip_rows, canvas_cols, False), 0.0
    )
    unit_norm, inv_std = layer_norm(convolved)
    normed = unit_norm.astype(jnp.bfloat16)
    tokens = normed.reshape(images * strip_rows * canvas_cols, channels)
    cot_rows = masked_cot.reshape(images * strip_rows * canvas_cols, channels)

    pre_act = jnp.dot(tokens, up_full, preferred_element_type=jnp.float32)
    hidden, derivative = gelu_parts(pre_act)
    activation = hidden.astype(jnp.bfloat16)
    blocks = 128
    down_term = lax.dot_general(
        activation.reshape(activation.shape[0], blocks, -1), cot_rows, (((0,), (0,)), ((), ())), preferred_element_type=jnp.float32
    )
    down_grad = reduce_weight_grad(down_term * grad_scale, ("c", "y", "z", "xl"))
    branch = jnp.dot(activation, down_full, preferred_element_type=jnp.float32)
    grad_act = lax.dot_general(
        cot_rows, down_full, (((1,), (1,)), ((), ())), preferred_element_type=jnp.float32
    )
    grad_pre = (grad_act * derivative).astype(jnp.bfloat16)
    up_term = lax.dot_general(
        tokens.reshape(tokens.shape[0], blocks, -1), grad_pre, (((0,), (0,)), ((), ())), preferred_element_type=jnp.float32
    )
    up_grad = reduce_weight_grad(up_term * grad_scale, ("c", "z", "y", "xl"))
    grad_rows = lax.dot_general(
        grad_pre, up_full, (((1,), (1,)), ((), ())), preferred_element_type=jnp.float32
    )

    branch = branch.reshape(features.shape)
    grad_norm = grad_rows.reshape(features.shape)
    block_out = (masked + branch).astype(jnp.bfloat16)
    grad_conv = jnp.where(inside_cells, norm_backward(grad_norm, unit_norm, inv_std), 0.0)
    kernel_grad = butterfly_sum(kernel_terms(grad_conv, padded, kernel.shape[0]) * grad_scale)
    grad_rimmed = padded_2(grad_conv.astype(jnp.bfloat16), (("rows", 1),), reach).astype(
        grad_conv.dtype
    )
    grad_padded = jnp.pad(grad_rimmed, ((0, 0), (0, 0), (reach, reach), (0, 0)))
    feature_grad = jnp.where(
        inside_cells,
        masked_cot + depthwise(grad_padded, kernel, strip_rows, canvas_cols, True),
        0.0,
    ).astype(jnp.bfloat16)
    return (block_out, feature_grad, up_grad, down_grad, kernel_grad)


def solution(mesh):
    torus = Mesh(mesh.devices.reshape(SIZES), AXES)
    strips = P(DP, "rows", None, None)
    return jax.shard_map(
        on_device,
        mesh=torus,
        in_specs=(strips, P(DP), P(), P(DP, None), P(DP, None), strips),
        out_specs=(strips, strips, P(DP, None), P(DP, None), P()),
        check_vma=False,
    )
```

```python
import jax
import jax.numpy as jnp
from jax import lax
from jax.sharding import Mesh
from jax.sharding import PartitionSpec as P

INV_ROOT_TWO = 0.7071067811865476
INV_ROOT_TAU = 0.3989422804014327
EPSILON = 1e-06

AXES = ("y", "z", "xl", "c", "rows")
SIZES = (4, 8, 2, 2, 2)
DP = AXES[:4]
SIZE = dict(zip(AXES, SIZES))


def ring_scatter(x, axis, wire):
    n = SIZE[axis]
    me = lax.axis_index(axis)
    dim = AXES.index(axis)
    d = 1
    while d < n:
        shape = list(x.shape)
        shape[dim : dim + 1] = [shape[dim] // 2, 2]
        pairs = x.reshape(shape)
        bit = (me // d) % 2
        keep = lax.dynamic_index_in_dim(pairs, bit, dim + 1, keepdims=False)
        send = lax.dynamic_index_in_dim(pairs, 1 - bit, dim + 1, keepdims=False)
        got = lax.ppermute(send.astype(wire), axis, [(i, i ^ d) for i in range(n)])
        x = keep + got.astype(jnp.float32)
        d *= 2
    return x


def ring_gather_rows(x, axis):
    n = SIZE[axis]
    me = lax.axis_index(axis)
    m = x.shape[0]
    out = jnp.zeros((n * m,) + x.shape[1:], x.dtype)
    out = lax.dynamic_update_slice_in_dim(out, x, me * m, 0)
    right = n // 2
    left = n - 1 - right
    cur = x
    for s in range(1, right + 1):
        cur = lax.ppermute(cur, axis, [(i, (i + 1) % n) for i in range(n)])
        out = lax.dynamic_update_slice_in_dim(out, cur, ((me - s) % n) * m, 0)
    cur = x
    for s in range(1, left + 1):
        cur = lax.ppermute(cur, axis, [(i, (i - 1) % n) for i in range(n)])
        out = lax.dynamic_update_slice_in_dim(out, cur, ((me + s) % n) * m, 0)
    return out


def gather_weights(up_shard, down_shard):
    lanes = 128
    packed = jnp.concatenate([up_shard.reshape(-1, lanes), down_shard.reshape(-1, lanes)])
    half = up_shard.size // lanes
    for axis in ("c", "xl", "y", "z"):
        packed = ring_gather_rows(packed, axis)
    packed = packed.reshape(SIZE["z"], SIZE["y"], -1, packed.shape[0] // 128, lanes)
    packed = packed.transpose(1, 0, 2, 3, 4).reshape(128, -1, lanes)
    up_full = packed[:, :half].reshape(-1, up_shard.shape[1])
    down_full = packed[:, half:].reshape(-1, down_shard.shape[1])
    return up_full, down_full


def reduce_weight_grad(term, order):
    rows = term.shape[0] // 128
    view = term.reshape(*SIZES[:4], 1, rows, term.shape[1])
    for axis in order:
        view = ring_scatter(view, axis, jnp.bfloat16)
    tiles = view.reshape(rows, term.shape[1])
    return tiles + lax.ppermute(tiles, "rows", [(0, 1), (1, 0)])


def butterfly_sum(x):
    for axis, n in zip(AXES, SIZES):
        d = 1
        while d < n:
            x = x + lax.ppermute(x, axis, [(i, i ^ d) for i in range(n)])
            d *= 2
    return x


def padded_2(block, sides, width):
    for axis, dim in sides:
        count = lax.axis_size(axis)
        forward = [(i, i + 1) for i in range(count - 1)]
        backward = [(target, source) for source, target in forward]
        low = lax.ppermute(
            lax.slice_in_dim(block, block.shape[dim] - width, None, axis=dim), axis, forward
        )
        high = lax.ppermute(lax.slice_in_dim(block, 0, width, axis=dim), axis, backward)
        block = jnp.concatenate([low, block, high], axis=dim)
    return block


def gelu_parts(pre_act):
    normal_cdf = 0.5 * (1.0 + lax.erf(pre_act * INV_ROOT_TWO))
    density = jnp.exp(-0.5 * pre_act * pre_act) * INV_ROOT_TAU
    return (pre_act * normal_cdf, normal_cdf + pre_act * density)


def depthwise(padded, kernel, out_rows, out_cols, flipped):
    span = kernel.shape[0]
    result = jnp.zeros(padded.shape[:-3] + (out_rows, out_cols, padded.shape[-1]), jnp.float32)
    for offset_row in range(span):
        for offset_col in range(span):
            start_row = span - 1 - offset_row if flipped else offset_row
            start_col = span - 1 - offset_col if flipped else offset_col
            result = (
                result
                + kernel[offset_row, offset_col]
                * padded[..., start_row : start_row + out_rows, start_col : start_col + out_cols, :]
            )
    return result


def kernel_terms(grad_conv, padded, span):
    reduce_axes = tuple(range(grad_conv.ndim - 1))
    rows_out = grad_conv.shape[-3]
    cols_out = grad_conv.shape[-2]
    kernel_rows = []
    for offset_row in range(span):
        kernel_row = []
        for offset_col in range(span):
            window = padded[
                ..., offset_row : offset_row + rows_out, offset_col : offset_col + cols_out, :
            ]
            kernel_row.append(jnp.sum(grad_conv * window, axis=reduce_axes))
        kernel_rows.append(jnp.stack(kernel_row))
    return jnp.stack(kernel_rows)


def layer_norm(convolved):
    centered = convolved - jnp.mean(convolved, axis=-1, keepdims=True)
    inv_std = lax.rsqrt(jnp.mean(centered * centered, axis=-1, keepdims=True) + EPSILON)
    return (centered * inv_std, inv_std)


def norm_backward(grad_norm, unit_norm, inv_std):
    first_mean = jnp.mean(grad_norm, axis=-1, keepdims=True)
    second_mean = jnp.mean(grad_norm * unit_norm, axis=-1, keepdims=True)
    return inv_std * (grad_norm - first_mean - unit_norm * second_mean)


def on_device(features, bucket, kernel, up_weight, down_weight, cotangent):
    images, strip_rows, canvas_cols, channels = features.shape
    rows_count = lax.axis_size("rows")
    row_index = lax.axis_index("rows")
    canvas_rows = strip_rows * rows_count
    area_cells = canvas_rows * canvas_cols // 2
    reach = kernel.shape[0] // 2
    grad_scale = 1.0 / (images * lax.axis_size(DP))
    heights = canvas_rows // 2 + bucket
    widths = jnp.minimum(canvas_cols, area_cells // heights)
    row_ids = row_index * strip_rows + lax.iota(jnp.int32, strip_rows)
    col_ids = lax.iota(jnp.int32, canvas_cols)
    inside = (row_ids[None, :, None] < heights[:, None, None]) & (
        col_ids[None, None, :] < widths[:, None, None]
    )
    inside_cells = inside[..., None]
    masked = jnp.where(inside_cells, features, jnp.zeros((), features.dtype))
    masked_cot = jnp.where(inside_cells, cotangent, jnp.zeros((), cotangent.dtype))
    up_full, down_full = gather_weights(up_weight, down_weight)
    rimmed = padded_2(masked, (("rows", 1),), reach)
    padded = jnp.pad(rimmed, ((0, 0), (0, 0), (reach, reach), (0, 0)))
    convolved = jnp.where(
        inside_cells, depthwise(padded, kernel, strip_rows, canvas_cols, False), 0.0
    )
    unit_norm, inv_std = layer_norm(convolved)
    normed = unit_norm.astype(jnp.bfloat16)
    tokens = normed.reshape(images * strip_rows * canvas_cols, channels)
    cot_rows = masked_cot.reshape(images * strip_rows * canvas_cols, channels)

    pre_act = jnp.dot(tokens, up_full, preferred_element_type=jnp.float32)
    hidden, derivative = gelu_parts(pre_act)
    activation = hidden.astype(jnp.bfloat16)
    down_term = lax.dot_general(
        activation, cot_rows, (((0,), (0,)), ((), ())), preferred_element_type=jnp.float32
    )
    down_grad = reduce_weight_grad(down_term * grad_scale, ("c", "y", "z", "xl"))
    branch = jnp.dot(activation, down_full, preferred_element_type=jnp.float32)
    grad_act = lax.dot_general(
        cot_rows, down_full, (((1,), (1,)), ((), ())), preferred_element_type=jnp.float32
    )
    grad_pre = (grad_act * derivative).astype(jnp.bfloat16)
    up_term = lax.dot_general(
        tokens, grad_pre, (((0,), (0,)), ((), ())), preferred_element_type=jnp.float32
    )
    up_grad = reduce_weight_grad(up_term * grad_scale, ("c", "z", "y", "xl"))
    grad_rows = lax.dot_general(
        grad_pre, up_full, (((1,), (1,)), ((), ())), preferred_element_type=jnp.float32
    )

    branch = branch.reshape(features.shape)
    grad_norm = grad_rows.reshape(features.shape)
    block_out = (masked + branch).astype(jnp.bfloat16)
    grad_conv = jnp.where(inside_cells, norm_backward(grad_norm, unit_norm, inv_std), 0.0)
    kernel_grad = butterfly_sum(kernel_terms(grad_conv, padded, kernel.shape[0]) * grad_scale)
    grad_rimmed = padded_2(grad_conv.astype(jnp.bfloat16), (("rows", 1),), reach).astype(
        grad_conv.dtype
    )
    grad_padded = jnp.pad(grad_rimmed, ((0, 0), (0, 0), (reach, reach), (0, 0)))
    feature_grad = jnp.where(
        inside_cells,
        masked_cot + depthwise(grad_padded, kernel, strip_rows, canvas_cols, True),
        0.0,
    ).astype(jnp.bfloat16)
    return (block_out, feature_grad, up_grad, down_grad, kernel_grad)


def solution(mesh):
    torus = Mesh(mesh.devices.reshape(SIZES), AXES)
    strips = P(DP, "rows", None, None)
    return jax.shard_map(
        on_device,
        mesh=torus,
        in_specs=(strips, P(DP), P(), P(DP, None), P(DP, None), strips),
        out_specs=(strips, strips, P(DP, None), P(DP, None), P()),
        check_vma=False,
    )
```
